128 devices in a mesh: expert: 16 (over y, x_lo, core), tensor: 8 (over x_hi, z).
Axes of the slice: x: 4 (x_hi: 2, x_lo: 2; x = x_hi * 2 + x_lo), y: 4, z: 4, core: 2. Of those that a mesh axis runs over, the one named last changes fastest.
Arguments:
- slot_choices: int32 [4096, 4], P('expert'), may hold values from 0 to 31, all different within a row; in each aligned block of 256 rows (0 to 255, 256 to 511, ...) at most 40 rows name the same one
- mix_weights: float32 [4096, 4], P('expert'), may hold values from 0.1 to 2.5
- tokens: bfloat16 [4096, 3584], P('expert'), may hold values from -6 to 6
- cotangent: bfloat16 [4096, 3584], P('expert'), may hold values from -0.71875 to 0.71875
- hot_experts: int32 [2], replicated, may hold values from 0 to 15, as said below
- replica_of: int32 [16], replicated, may hold values from 0 to 15, as said below
- weights_in: bfloat16 [16, 2, 3584, 1024], P('expert', None, None, 'tensor'), may hold values from -0.1796875 to 0.1796875
- weights_down: bfloat16 [16, 1024, 3584], P('expert', 'tensor'), may hold values from -0.1796875 to 0.1796875
- mean_in: bfloat16 [16, 2, 3584, 1024], P('expert', None, None, 'tensor'), may hold values from -1.796875 to 1.796875
- mean_down: bfloat16 [16, 1024, 3584], P('expert', 'tensor'), may hold values from -1.796875 to 1.796875
- square_in: bfloat16 [16, 2, 3584, 1024], P('expert', None, None, 'tensor'), may hold values from 0.099609375 to 1
- square_down: bfloat16 [16, 1024, 3584], P('expert', 'tensor'), may hold values from 0.099609375 to 1
Outputs:
- stepped_in: bfloat16 [16, 2, 3584, 1024], P('expert', None, None, 'tensor')
- stepped_down: bfloat16 [16, 1024, 3584], P('expert', 'tensor')
- averaged_in: bfloat16 [16, 2, 3584, 1024], P('expert', None, None, 'tensor')
- averaged_down: bfloat16 [16, 1024, 3584], P('expert', 'tensor')
- squared_in: bfloat16 [16, 2, 3584, 1024], P('expert', None, None, 'tensor')
- squared_down: bfloat16 [16, 1024, 3584], P('expert', 'tensor')
- copied_in: bfloat16 [16, 2, 3584, 1024], P('expert', None, None, 'tensor')
- copied_down: bfloat16 [16, 1024, 3584], P('expert', 'tensor')
The draws below stay inside these ranges and needn't reach their ends.
Inputs may be any that keep to these rules, and one draw needn't show every extreme that they name: `slot_choices`: within the 256 tokens of one index of expert, no slot is named by more than 40 choices; the 4 slots of one token differ. `hot_experts`: 2 different experts, one of them expert 16 - 1. `replica_of`: entry j is one of hot_experts and never j; each of hot_experts is named by some entry.
All inputs are finite; a program needn't handle non-finite values.
Results may differ from the reference program's by a relative error of at most 0.023.
Values may be sent and summed in bfloat16 or wider, within the bound.
No kernel may reach another device: no remote copies, remote signals or barrier semaphores. Data moves between devices by JAX's collectives and lax.ppermute only.
A program may use at most 192 MiB of HBM per device.

```python
import math
import jax
import jax.numpy as jnp
import numpy as np
from jax import lax

D = 3584
FF = 1024
TOP = 4
HOT = 2
TOK_DEV = 256
EXPERTS = 16
SLOTS = 32
TOKENS = 4096
CAP = 40


def hot_choice(key):
    others = jax.random.permutation(jax.random.fold_in(key, 7), EXPERTS - 1)[:HOT - 1].astype(jnp.int32)
    joined = jnp.concatenate([others, jnp.full((1,), EXPERTS - 1, jnp.int32)])
    order = jax.random.permutation(jax.random.fold_in(key, 13), HOT)
    return joined[order].astype(jnp.int32)


def draw_hot_experts(key, part):
    return hot_choice(key)


def draw_replica_of(key, part):
    chosen = hot_choice(key)
    picks = jax.random.randint(jax.random.fold_in(key, 11), (EXPERTS,), 0, HOT)
    first_pick = chosen[picks]
    second_pick = chosen[(picks + 1) % HOT]
    devices = jnp.arange(EXPERTS, dtype=jnp.int32)
    plan = jnp.where(first_pick == devices, second_pick, first_pick)
    plan = plan.at[chosen[0]].set(chosen[1])
    plan = plan.at[chosen[1]].set(chosen[0])
    return plan.astype(jnp.int32)


def block_scale(key, shape, cuts, smallest, high):
    loudness = 1.0
    for dim, blocks in cuts:
        steps = jax.random.uniform(jax.random.fold_in(jax.random.fold_in(key, 6), dim), (blocks,), jnp.float32, smallest / len(cuts), high / len(cuts))
        loudness = loudness * jnp.repeat(jnp.exp(steps), shape[dim] // blocks).reshape((-1,) + (1,) * (len(shape) - 1 - dim))
    return loudness


def deal_out(stream_key, own, number, rows, count, top, most, slope):
    ranking = jax.random.permutation(stream_key, count)
    packed, common = load_shares(count, rows * top, most, slope, True), load_shares(count, rows * top, most, slope, False)
    places = jnp.arange(count)

    def named(tallies, offset_by):
        used = int((tallies > 0).sum())
        fixed = max(1, used // 4)
        shifted = fixed + (places - fixed + offset_by * (used - fixed)) % max(1, count - fixed)
        return jnp.zeros((count,), jnp.int32).at[ranking[jnp.where(places < fixed, places, shifted)]].set(jnp.asarray(tallies, jnp.int32))

    tallies = jnp.where(number % 4 == 0, named(packed, number // 4), named(common, number - number // 4 - 1))
    mixed = jax.random.permutation(jax.random.fold_in(own, 3), count)
    giver, taker = mixed[0:count // 2 * 2:2], mixed[1:count // 2 * 2:2]
    margin = jnp.minimum(tallies[giver] - 1, most - tallies[taker]) // 2
    margin = jnp.where((giver == ranking[0]) | (taker == ranking[0]) | (tallies[taker] == 0), 0, jnp.maximum(margin, 0))
    shifted = jax.random.randint(jax.random.fold_in(own, 4), (count // 2,), 0, 1 << 20) % (margin + 1)
    tallies = tallies.at[giver].add(-shifted).at[taker].add(shifted)
    labels = jnp.searchsorted(jnp.cumsum(tallies), jnp.arange(rows * top), side="right").astype(jnp.int32)
    table = labels.reshape(top, rows).T
    table = table[jax.random.permutation(jax.random.fold_in(own, 1), rows)]
    offset_by = jax.random.randint(jax.random.fold_in(own, 2), (rows, 1), 0, top)
    return jnp.take_along_axis(table, (jnp.arange(top)[None, :] + offset_by) % top, axis=1)


def load_shares(amount, total, most, lean, full):
    weights = [(1 << 20) // math.isqrt(rank ** lean) + 1 for rank in range(1, amount + 1)]
    largest = most if full else min(most, max(-(-total // amount), total * weights[0] // sum(weights)))
    least = 1 if total - largest >= amount - 1 else 0
    given, surplus = [largest] + [least] * (amount - 1), total - largest - least * (amount - 1)
    while surplus > 0:
        movable = [i for i in range(1, amount) if given[i] < largest] or [i for i in range(1, amount) if given[i] < most]
        pool, remaining = sum([weights[i] for i in movable]), surplus
        for i in movable:
            addition = min(most - given[i], max(1, remaining * weights[i] // pool), surplus)
            given[i] = given[i] + addition
            surplus = surplus - addition
    return np.array(given)


def normal_values(own_key, dims, width, limit, pieces=(), kind=jnp.bfloat16):
    loudness = block_scale(own_key, dims, pieces, -0.22, 0.18) if pieces else 1.0
    drawn = jax.random.normal(own_key, dims, jnp.float32) * width * loudness
    return jnp.minimum(jnp.maximum(drawn, -limit), limit).astype(kind)


def setup_inputs(seed: int = 0) -> dict:
    arg_keys = jax.random.split(jax.random.key(seed), 13)
    slot_choices_keys = jax.random.split(jax.random.fold_in(arg_keys[0], 1), TOKENS // TOK_DEV)
    slot_choices_turns = jax.random.permutation(jax.random.fold_in(arg_keys[0], 3), TOKENS // TOK_DEV)
    slot_choices = jax.vmap(lambda own, number: deal_out(jax.random.fold_in(arg_keys[0], 2), own, number, TOK_DEV, SLOTS, TOP, CAP, 2))(slot_choices_keys, slot_choices_turns).reshape((TOKENS, TOP))
    mix_weights = jnp.clip(jnp.exp(math.log(2.5) - 3.218876 * jax.random.uniform(arg_keys[1], (TOKENS, TOP), jnp.float32) ** block_scale(arg_keys[1], (TOKENS, TOP), ((0, 16),), -0.2, 0.2)), 0.1, 2.5)
    tokens = normal_values(arg_keys[2], (TOKENS, D), 1.0, 6.0, ((0, 16),))
    cotangent = normal_values(arg_keys[3], (TOKENS, D), 0.12, 0.71875, ((0, 16),))
    hot_experts = draw_hot_experts(jax.random.fold_in(arg_keys[12], 71), 0)
    replica_of = draw_replica_of(jax.random.fold_in(arg_keys[12], 71), 0)
    weights_in = normal_values(arg_keys[6], (EXPERTS, 2, D, FF), 0.03, 0.1796875, ((0, 16), (3, 8)))
    weights_down = normal_values(arg_keys[7], (EXPERTS, FF, D), 0.03, 0.1796875, ((0, 16), (1, 8)))
    mean_in = normal_values(arg_keys[8], (EXPERTS, 2, D, FF), 0.3, 1.796875, ((0, 16), (3, 8)))
    mean_down = normal_values(arg_keys[9], (EXPERTS, FF, D), 0.3, 1.796875, ((0, 16), (1, 8)))
    square_in = jnp.clip(jnp.exp(math.log(1.0) - 2.306499 * jax.random.uniform(arg_keys[10], (EXPERTS, 2, D, FF), jnp.float32) ** block_scale(arg_keys[10], (EXPERTS, 2, D, FF), ((0, 16), (3, 8)), -0.2, 0.2)), 0.099609375, 1.0).astype(jnp.bfloat16)
    square_down = jnp.clip(jnp.exp(math.log(1.0) - 2.306499 * jax.random.uniform(arg_keys[11], (EXPERTS, FF, D), jnp.float32) ** block_scale(arg_keys[11], (EXPERTS, FF, D), ((0, 16), (1, 8)), -0.2, 0.2)), 0.099609375, 1.0).astype(jnp.bfloat16)
    return {"slot_choices": slot_choices, "mix_weights": mix_weights, "tokens": tokens, "cotangent": cotangent, "hot_experts": hot_experts, "replica_of": replica_of, "weights_in": weights_in, "weights_down": weights_down, "mean_in": mean_in, "mean_down": mean_down, "square_in": square_in, "square_down": square_down}


beta_one = 0.9
beta_two = 0.95
learn_rate = 0.02
decay_rate = 0.1
epsilon = 1e-08
weight_scale = 0.03

def adam_step(weight, moment_one, moment_two, gradient):
    first_new = beta_one * moment_one.astype(jnp.float32) + (1.0 - beta_one) * gradient
    second_new = beta_two * moment_two.astype(jnp.float32) + (1.0 - beta_two) * gradient * gradient
    base_val = weight.astype(jnp.float32)
    weight_new = base_val - learn_rate * (first_new / (jnp.sqrt(second_new) + epsilon) + decay_rate * base_val)
    return (weight_new.astype(jnp.bfloat16), first_new.astype(jnp.bfloat16), second_new.astype(jnp.bfloat16))

def slot_partial(slot_value, expert_id, slot_choices, mix_weights, tokens, cotangent, weights_in, weights_down):
    flat_ids = slot_choices.reshape(-1)
    limit_rows = EXPERTS * CAP
    matches = flat_ids == slot_value
    picked = jnp.nonzero(matches, size=limit_rows, fill_value=0)[0].astype(jnp.int32)
    present = jnp.arange(limit_rows, dtype=jnp.int32) < jnp.sum(matches.astype(jnp.int32))
    token_index = picked // TOP
    rows_token = jnp.where(present[:, None], tokens[token_index], jnp.zeros((), tokens.dtype))
    scaled = jnp.where(present, mix_weights.reshape(-1)[picked], 0.0)
    rows_cotan = (scaled[:, None] * cotangent[token_index].astype(jnp.float32)).astype(jnp.bfloat16)
    weight_in = weights_in[expert_id]
    weight_down = weights_down[expert_id]
    scale_in = 1.0 / (weight_scale * D ** 0.5)
    scale_down = 1.0 / (weight_scale * FF ** 0.5)
    gate_val = jnp.dot(rows_token, weight_in[0], preferred_element_type=jnp.float32) * scale_in
    up_val = jnp.dot(rows_token, weight_in[1], preferred_element_type=jnp.float32) * scale_in
    sigmoid_val = jax.nn.sigmoid(gate_val)
    active = gate_val * sigmoid_val
    hidden = (active * up_val).astype(jnp.bfloat16)
    back_grad = jnp.dot(rows_cotan, weight_down.T, preferred_element_type=jnp.float32) * scale_down
    slope_gate = (back_grad * up_val * sigmoid_val * (1.0 + gate_val * (1.0 - sigmoid_val))).astype(jnp.bfloat16)
    slope_up = (back_grad * active).astype(jnp.bfloat16)
    part_in = jnp.stack([jnp.dot(rows_token.T, slope_gate, preferred_element_type=jnp.float32), jnp.dot(rows_token.T, slope_up, preferred_element_type=jnp.float32)]) * scale_in
    part_down = jnp.dot(hidden.T, rows_cotan, preferred_element_type=jnp.float32) * scale_down
    return (part_in, part_down)

def rounded(value):
    return lax.optimization_barrier(value.astype(jnp.bfloat16)).astype(jnp.float32)

def reference(slot_choices, mix_weights, tokens, cotangent, hot_experts, replica_of, weights_in, weights_down, mean_in, mean_down, square_in, square_down):

    def partial_of(slot_value, expert_id):
        return slot_partial(slot_value, expert_id, slot_choices, mix_weights, tokens, cotangent, weights_in, weights_down)

    def one_expert(expert_id):
        own_in, own_down = partial_of(2 * expert_id, expert_id)

        def add_copy(index, totals):

            def compute(operand_in):
                part_in, part_down = partial_of(2 * index + 1, expert_id)
                return (rounded(part_in), rounded(part_down))

            def skipped(operand_in):
                return (jnp.zeros_like(own_in), jnp.zeros_like(own_down))
            extra_in, extra_down = lax.cond(replica_of[index] == expert_id, compute, skipped, 0)
            return (totals[0] + extra_in, totals[1] + extra_down)
        hot_in, hot_down = lax.fori_loop(0, EXPERTS, add_copy, (rounded(own_in), rounded(own_down)))
        is_hot = jnp.any(hot_experts == expert_id)
        grad_in = jnp.where(is_hot, hot_in, own_in)
        grad_down = jnp.where(is_hot, hot_down, own_down)
        new_in = adam_step(weights_in[expert_id], mean_in[expert_id], square_in[expert_id], grad_in)
        new_down = adam_step(weights_down[expert_id], mean_down[expert_id], square_down[expert_id], grad_down)
        return (new_in[0], new_down[0], new_in[1], new_down[1], new_in[2], new_down[2])
    results = lax.map(one_expert, jnp.arange(EXPERTS, dtype=jnp.int32))
    stepped_in, stepped_down, averaged_in, averaged_down, squared_in, squared_down = results
    copied_in = stepped_in[replica_of]
    copied_down = stepped_down[replica_of]
    return (stepped_in, stepped_down, averaged_in, averaged_down, squared_in, squared_down, copied_in, copied_down)
```

```python
import math

import jax
import jax.numpy as jnp
from jax import lax
from jax.sharding import PartitionSpec as P

beta_one = 0.9
beta_two = 0.95
learn_rate = 0.02
decay_rate = 0.1
epsilon = 1e-08
weight_scale = 0.03


def broadcast(block, axis, source):
    block = jnp.where(lax.axis_index(axis) == source, block, jnp.zeros_like(block))
    return lax.psum(block, axis)


def adam_step(weight, moment_one, moment_two, gradient):
    first_new = beta_one * moment_one.astype(jnp.float32) + (1.0 - beta_one) * gradient
    second_new = beta_two * moment_two.astype(jnp.float32) + (1.0 - beta_two) * gradient * gradient
    base_val = weight.astype(jnp.float32)
    weight_new = base_val - learn_rate * (
        first_new / (jnp.sqrt(second_new) + epsilon) + decay_rate * base_val
    )
    return (
        weight_new.astype(jnp.bfloat16),
        first_new.astype(jnp.bfloat16),
        second_new.astype(jnp.bfloat16),
    )


def build_rows(slot_choices, mix_weights, tokens, cotangent, slot_count, capacity, row_count):
    top_count = slot_choices.shape[1]
    flat_ids = slot_choices.reshape(-1)
    entries = flat_ids.shape[0]
    onehot = (flat_ids[:, None] == jnp.arange(slot_count, dtype=jnp.int32)[None, :]).astype(
        jnp.int32
    )
    before = jnp.cumsum(onehot, axis=0) - onehot
    position = jnp.sum(before * onehot, axis=1)
    target = flat_ids * capacity + position
    wanted = (
        jnp.arange(slot_count, dtype=jnp.int32)[:, None] * capacity
        + jnp.arange(row_count, dtype=jnp.int32)[None, :]
    ).reshape(-1)
    matches = wanted[:, None] == target[None, :]
    present = jnp.any(matches, axis=1)
    source = jnp.sum(jnp.where(matches, jnp.arange(entries, dtype=jnp.int32)[None, :], 0), axis=1)
    token_index = source // top_count
    rows_token = jnp.where(present[:, None], tokens[token_index], jnp.zeros((), tokens.dtype))
    weight = jnp.where(present, mix_weights.reshape(-1)[source], 0.0)
    rows_cotan = (weight[:, None] * cotangent[token_index].astype(jnp.float32)).astype(jnp.bfloat16)
    row_shape = (slot_count // 2, 2, row_count, tokens.shape[1])
    return (rows_token.reshape(row_shape), rows_cotan.reshape(row_shape))


def slot_terms(rows_token, rows_cotan, weight_in, weight_down, scale_in, scale_down):
    joined = (
        jnp.einsum("rd,gdf->grf", rows_token, weight_in, preferred_element_type=jnp.float32)
        * scale_in
    )
    gate_val = joined[0]
    up_val = joined[1]
    sigmoid_val = jax.nn.sigmoid(gate_val)
    active = gate_val * sigmoid_val
    hidden = (active * up_val).astype(jnp.bfloat16)
    back_grad = (
        jnp.einsum("rd,fd->rf", rows_cotan, weight_down, preferred_element_type=jnp.float32)
        * scale_down
    )
    slope_gate = (back_grad * up_val * sigmoid_val * (1.0 + gate_val * (1.0 - sigmoid_val))).astype(
        jnp.bfloat16
    )
    slope_up = (back_grad * active).astype(jnp.bfloat16)
    slopes = jnp.stack([slope_gate, slope_up])
    grad_in = jnp.einsum("rd,grf->gdf", rows_token, slopes, preferred_element_type=jnp.float32)
    grad_down = jnp.einsum("rf,rd->fd", hidden, rows_cotan, preferred_element_type=jnp.float32)
    return (grad_in, grad_down)


def pack(part_in, part_down, groups):
    width = part_in.shape[1]
    inner = part_in.shape[2]
    return jnp.concatenate(
        [
            part_in.reshape(groups, 2 * width // groups, inner),
            part_down.reshape(groups, width // groups, inner),
        ],
        axis=1,
    )


def unpack(packed, width, inner):
    groups = packed.shape[0]
    split = 2 * width // groups
    part_in = packed[:, :split].reshape(2, width, inner)
    part_down = packed[:, split:].reshape(inner, width)
    return part_in, part_down


def exchange(block):
    return lax.all_to_all(block, "expert", 0, 0, tiled=True)


def spread_hot(packed, hot_experts, replica_of):
    arrived = exchange(packed)
    first = lax.dynamic_index_in_dim(arrived, hot_experts[0], 0, keepdims=False)
    second = lax.dynamic_index_in_dim(arrived, hot_experts[1], 0, keepdims=False)
    wants_first = (replica_of == hot_experts[0])[:, None, None]
    outgoing = jnp.where(wants_first, first[None], second[None])
    return exchange(outgoing)


def body(
    slot_choices,
    mix_weights,
    tokens,
    cotangent,
    hot_experts,
    replica_of,
    weights_in,
    weights_down,
    mean_in,
    mean_down,
    square_in,
    square_down,
):
    expert_count = lax.axis_size("expert")
    tensor_count = lax.axis_size("tensor")
    token_count = slot_choices.shape[0]
    top_count = slot_choices.shape[1]
    share = (5 * token_count * top_count + 8 * expert_count * tensor_count - 1) // (
        8 * expert_count * tensor_count
    )
    capacity = share * tensor_count
    own_index = lax.axis_index("expert")
    own_in = weights_in[0]
    own_down = weights_down[0]
    width = tokens.shape[1]
    inner = own_in.shape[2]
    scale_in = 1.0 / (weight_scale * math.sqrt(width))
    scale_down = 1.0 / (weight_scale * math.sqrt(inner * tensor_count))
    held_in, held_down = unpack(
        spread_hot(pack(own_in, own_down, expert_count), hot_experts, replica_of), width, inner
    )
    weight_sets = ((own_in, own_down), (held_in, held_down))
    built_token, built_cotan = build_rows(
        slot_choices, mix_weights, tokens, cotangent, 2 * expert_count, capacity, capacity
    )
    recv_token, recv_cotan = (
        lax.all_to_all(built_token, "expert", split_axis=0, concat_axis=0, tiled=True),
        lax.all_to_all(built_cotan, "expert", split_axis=0, concat_axis=0, tiled=True),
    )
    result = []
    for add_which in range(2):
        part_in, part_down = slot_terms(
            recv_token[:, add_which].reshape(-1, width),
            recv_cotan[:, add_which].reshape(-1, width),
            weight_sets[add_which][0],
            weight_sets[add_which][1],
            scale_in,
            scale_down,
        )
        result.append(part_in)
        result.append(part_down)
    totals = tuple(result)
    grad_in = totals[0] * scale_in
    grad_down = totals[1] * scale_down
    copy_in = totals[2] * scale_in
    copy_down = totals[3] * scale_down
    copy_packed = pack(
        copy_in.astype(jnp.bfloat16), copy_down.astype(jnp.bfloat16), expert_count
    )
    arrived = exchange(copy_packed).astype(jnp.float32)
    sources = jnp.arange(expert_count, dtype=jnp.int32)
    sums = []
    for which in range(2):
        picked = (replica_of == hot_experts[which])[:, None, None]
        sums.append(jnp.sum(jnp.where(picked, arrived, 0.0), axis=0))
    to_owner = jnp.where(
        (sources == hot_experts[0])[:, None, None],
        sums[0][None],
        jnp.where((sources == hot_experts[1])[:, None, None], sums[1][None], 0.0),
    ).astype(jnp.bfloat16)
    gathered_in, gathered_down = unpack(
        exchange(to_owner).astype(jnp.float32), width, inner
    )
    is_hot = jnp.any(hot_experts == own_index)
    total_in = jnp.where(
        is_hot, grad_in.astype(jnp.bfloat16).astype(jnp.float32) + gathered_in, grad_in
    )
    total_down = jnp.where(
        is_hot, grad_down.astype(jnp.bfloat16).astype(jnp.float32) + gathered_down, grad_down
    )
    stepped_in, averaged_in, squared_in = adam_step(own_in, mean_in[0], square_in[0], total_in)
    stepped_down, averaged_down, squared_down = adam_step(
        own_down, mean_down[0], square_down[0], total_down
    )
    copied_in, copied_down = unpack(
        spread_hot(pack(stepped_in, stepped_down, expert_count), hot_experts, replica_of),
        width,
        inner,
    )
    return (
        stepped_in[None],
        stepped_down[None],
        averaged_in[None],
        averaged_down[None],
        squared_in[None],
        squared_down[None],
        copied_in[None],
        copied_down[None],
    )


def solution(mesh):
    placed = (
        P("expert", None),
        P("expert", None),
        P("expert", None),
        P("expert", None),
        P(),
        P(),
        P("expert", None, None, "tensor"),
        P("expert", "tensor", None),
        P("expert", None, None, "tensor"),
        P("expert", "tensor", None),
        P("expert", None, None, "tensor"),
        P("expert", "tensor", None),
    )
    return jax.shard_map(
        body,
        mesh=mesh,
        in_specs=placed,
        out_specs=(
            P("expert", None, None, "tensor"),
            P("expert", "tensor", None),
            P("expert", None, None, "tensor"),
            P("expert", "tensor", None),
            P("expert", None, None, "tensor"),
            P("expert", "tensor", None),
            P("expert", None, None, "tensor"),
            P("expert", "tensor", None),
        ),
        check_vma=False,
    )
```

```python
import math

import jax
import jax.numpy as jnp
from jax import lax
from jax.sharding import PartitionSpec as P

beta_one = 0.9
beta_two = 0.95
learn_rate = 0.02
decay_rate = 0.1
epsilon = 1e-08
weight_scale = 0.03


def broadcast(block, axis, source):
    block = jnp.where(lax.axis_index(axis) == source, block, jnp.zeros_like(block))
    return lax.psum(block, axis)


def adam_step(weight, moment_one, moment_two, gradient):
    first_new = beta_one * moment_one.astype(jnp.float32) + (1.0 - beta_one) * gradient
    second_new = beta_two * moment_two.astype(jnp.float32) + (1.0 - beta_two) * gradient * gradient
    base_val = weight.astype(jnp.float32)
    weight_new = base_val - learn_rate * (
        first_new / (jnp.sqrt(second_new) + epsilon) + decay_rate * base_val
    )
    return (
        weight_new.astype(jnp.bfloat16),
        first_new.astype(jnp.bfloat16),
        second_new.astype(jnp.bfloat16),
    )


def build_rows(slot_choices, mix_weights, tokens, cotangent, slot_count, capacity, row_count):
    top_count = slot_choices.shape[1]
    flat_ids = slot_choices.reshape(-1)
    entries = flat_ids.shape[0]
    onehot = (flat_ids[:, None] == jnp.arange(slot_count, dtype=jnp.int32)[None, :]).astype(
        jnp.int32
    )
    before = jnp.cumsum(onehot, axis=0) - onehot
    position = jnp.sum(before * onehot, axis=1)
    target = flat_ids * capacity + position
    wanted = (
        jnp.arange(slot_count, dtype=jnp.int32)[:, None] * capacity
        + jnp.arange(row_count, dtype=jnp.int32)[None, :]
    ).reshape(-1)
    matches = wanted[:, None] == target[None, :]
    present = jnp.any(matches, axis=1)
    source = jnp.sum(jnp.where(matches, jnp.arange(entries, dtype=jnp.int32)[None, :], 0), axis=1)
    token_index = source // top_count
    rows_token = jnp.where(present[:, None], tokens[token_index], jnp.zeros((), tokens.dtype))
    weight = jnp.where(present, mix_weights.reshape(-1)[source], 0.0)
    rows_cotan = (weight[:, None] * cotangent[token_index].astype(jnp.float32)).astype(jnp.bfloat16)
    row_shape = (slot_count // 2, 2, row_count, tokens.shape[1])
    return (rows_token.reshape(row_shape), rows_cotan.reshape(row_shape))


def slot_terms(rows_token, rows_cotan, weight_in, weight_down, scale_in, scale_down):
    joined = (
        jnp.einsum("rd,gdf->grf", rows_token, weight_in, preferred_element_type=jnp.float32)
        * scale_in
    )
    gate_val = joined[0]
    up_val = joined[1]
    sigmoid_val = jax.nn.sigmoid(gate_val)
    active = gate_val * sigmoid_val
    hidden = (active * up_val).astype(jnp.bfloat16)
    back_grad = (
        jnp.einsum("rd,fd->rf", rows_cotan, weight_down, preferred_element_type=jnp.float32)
        * scale_down
    )
    slope_gate = (back_grad * up_val * sigmoid_val * (1.0 + gate_val * (1.0 - sigmoid_val))).astype(
        jnp.bfloat16
    )
    slope_up = (back_grad * active).astype(jnp.bfloat16)
    slopes = jnp.stack([slope_gate, slope_up])
    grad_in = jnp.einsum("rd,grf->gdf", rows_token, slopes, preferred_element_type=jnp.float32)
    grad_down = jnp.einsum("rf,rd->fd", hidden, rows_cotan, preferred_element_type=jnp.float32)
    return (grad_in, grad_down)


def pack(part_in, part_down, groups):
    width = part_in.shape[1]
    inner = part_in.shape[2]
    return jnp.concatenate(
        [
            part_in.reshape(groups, 2 * width // groups, inner),
            part_down.reshape(groups, width // groups, inner),
        ],
        axis=1,
    )


def unpack(packed, width, inner):
    groups = packed.shape[0]
    split = 2 * width // groups
    part_in = packed[:, :split].reshape(2, width, inner)
    part_down = packed[:, split:].reshape(inner, width)
    return part_in, part_down


def exchange(block):
    return lax.all_to_all(block, "expert", 0, 0, tiled=True)


def spread_hot(packed, hot_experts, replica_of):
    arrived = exchange(packed)
    first = lax.dynamic_index_in_dim(arrived, hot_experts[0], 0, keepdims=False)
    second = lax.dynamic_index_in_dim(arrived, hot_experts[1], 0, keepdims=False)
    wants_first = (replica_of == hot_experts[0])[:, None, None]
    outgoing = jnp.where(wants_first, first[None], second[None])
    return exchange(outgoing)


def body(
    slot_choices,
    mix_weights,
    tokens,
    cotangent,
    hot_experts,
    replica_of,
    weights_in,
    weights_down,
    mean_in,
    mean_down,
    square_in,
    square_down,
):
    expert_count = lax.axis_size("expert")
    tensor_count = lax.axis_size("tensor")
    token_count = slot_choices.shape[0]
    top_count = slot_choices.shape[1]
    share = (5 * token_count * top_count + 8 * expert_count * tensor_count - 1) // (
        8 * expert_count * tensor_count
    )
    capacity = share * tensor_count
    own_index = lax.axis_index("expert")
    own_in = weights_in[0]
    own_down = weights_down[0]
    width = tokens.shape[1]
    inner = own_in.shape[2]
    scale_in = 1.0 / (weight_scale * math.sqrt(width))
    scale_down = 1.0 / (weight_scale * math.sqrt(inner * tensor_count))
    own_packed = pack(own_in, own_down, expert_count)
    held_in, held_down = unpack(spread_hot(own_packed, hot_experts, replica_of), width, inner)
    weight_sets = ((own_in, own_down), (held_in, held_down))
    built_token, built_cotan = build_rows(
        slot_choices, mix_weights, tokens, cotangent, 2 * expert_count, capacity, capacity
    )
    def rows_of(add_which):
        outgoing = jnp.stack([built_token[:, add_which], built_cotan[:, add_which]], axis=1)
        return exchange(outgoing)

    def terms_of(arrived_rows, add_which):
        return slot_terms(
            arrived_rows[:, 0].reshape(-1, width),
            arrived_rows[:, 1].reshape(-1, width),
            weight_sets[add_which][0],
            weight_sets[add_which][1],
            scale_in,
            scale_down,
        )

    copy_rows = rows_of(1)
    copy_in, copy_down = terms_of(copy_rows, 1)
    own_rows = rows_of(0)
    copy_packed = pack(
        (copy_in * scale_in).astype(jnp.bfloat16),
        (copy_down * scale_down).astype(jnp.bfloat16),
        expert_count,
    )
    copy_packed, own_rows = lax.optimization_barrier((copy_packed, own_rows))
    grad_in, grad_down = terms_of(own_rows, 0)
    grad_in = grad_in * scale_in
    grad_down = grad_down * scale_down
    arrived = exchange(copy_packed).astype(jnp.float32)
    sources = jnp.arange(expert_count, dtype=jnp.int32)
    sums = []
    for which in range(2):
        picked = (replica_of == hot_experts[which])[:, None, None]
        sums.append(jnp.sum(jnp.where(picked, arrived, 0.0), axis=0))
    to_owner = jnp.where(
        (sources == hot_experts[0])[:, None, None],
        sums[0][None],
        jnp.where((sources == hot_experts[1])[:, None, None], sums[1][None], 0.0),
    ).astype(jnp.bfloat16)
    gathered = exchange(to_owner).astype(jnp.float32)
    is_hot = jnp.any(hot_experts == own_index)
    own_grad = pack(grad_in, grad_down, expert_count)
    total = jnp.where(is_hot, own_grad.astype(jnp.bfloat16).astype(jnp.float32) + gathered, own_grad)
    stepped_p, averaged_p, squared_p = adam_step(
        own_packed,
        pack(mean_in[0], mean_down[0], expert_count),
        pack(square_in[0], square_down[0], expert_count),
        total,
    )
    copied_in, copied_down = unpack(spread_hot(stepped_p, hot_experts, replica_of), width, inner)
    stepped_in, stepped_down = unpack(stepped_p, width, inner)
    averaged_in, averaged_down = unpack(averaged_p, width, inner)
    squared_in, squared_down = unpack(squared_p, width, inner)
    return (
        stepped_in[None],
        stepped_down[None],
        averaged_in[None],
        averaged_down[None],
        squared_in[None],
        squared_down[None],
        copied_in[None],
        copied_down[None],
    )


def solution(mesh):
    placed = (
        P("expert", None),
        P("expert", None),
        P("expert", None),
        P("expert", None),
        P(),
        P(),
        P("expert", None, None, "tensor"),
        P("expert", "tensor", None),
        P("expert", None, None, "tensor"),
        P("expert", "tensor", None),
        P("expert", None, None, "tensor"),
        P("expert", "tensor", None),
    )
    return jax.shard_map(
        body,
        mesh=mesh,
        in_specs=placed,
        out_specs=(
            P("expert", None, None, "tensor"),
            P("expert", "tensor", None),
            P("expert", None, None, "tensor"),
            P("expert", "tensor", None),
            P("expert", None, None, "tensor"),
            P("expert", "tensor", None),
            P("expert", None, None, "tensor"),
            P("expert", "tensor", None),
        ),
        check_vma=False,
    )
```

```python
import math

import jax
import jax.numpy as jnp
from jax import lax
from jax.sharding import PartitionSpec as P

beta_one = 0.9
beta_two = 0.95
learn_rate = 0.02
decay_rate = 0.1
epsilon = 1e-08
weight_scale = 0.03


def broadcast(block, axis, source):
    block = jnp.where(lax.axis_index(axis) == source, block, jnp.zeros_like(block))
    return lax.psum(block, axis)


def adam_step(weight, moment_one, moment_two, gradient):
    first_new = beta_one * moment_one.astype(jnp.float32) + (1.0 - beta_one) * gradient
    second_new = beta_two * moment_two.astype(jnp.float32) + (1.0 - beta_two) * gradient * gradient
    base_val = weight.astype(jnp.float32)
    weight_new = base_val - learn_rate * (
        first_new / (jnp.sqrt(second_new) + epsilon) + decay_rate * base_val
    )
    return (
        weight_new.astype(jnp.bfloat16),
        first_new.astype(jnp.bfloat16),
        second_new.astype(jnp.bfloat16),
    )


def route_rows(slot_choices, mix_weights, slot_count, capacity, row_count):
    top_count = slot_choices.shape[1]
    flat_ids = slot_choices.reshape(-1)
    entries = flat_ids.shape[0]
    onehot = (flat_ids[:, None] == jnp.arange(slot_count, dtype=jnp.int32)[None, :]).astype(
        jnp.int32
    )
    before = jnp.cumsum(onehot, axis=0) - onehot
    position = jnp.sum(before * onehot, axis=1)
    target = flat_ids * capacity + position
    wanted = (
        jnp.arange(slot_count, dtype=jnp.int32)[:, None] * capacity
        + jnp.arange(row_count, dtype=jnp.int32)[None, :]
    ).reshape(-1)
    matches = wanted[:, None] == target[None, :]
    present = jnp.any(matches, axis=1)
    source = jnp.sum(jnp.where(matches, jnp.arange(entries, dtype=jnp.int32)[None, :], 0), axis=1)
    weight = jnp.where(present, mix_weights.reshape(-1)[source], 0.0)
    return source // top_count, present, weight


def gather_rows(token_index, present, weight, tokens, cotangent, slot_count, row_count):
    rows_token = jnp.where(present[:, None], tokens[token_index], jnp.zeros((), tokens.dtype))
    rows_cotan = (weight[:, None] * cotangent[token_index].astype(jnp.float32)).astype(jnp.bfloat16)
    row_shape = (slot_count // 2, 2, row_count, tokens.shape[1])
    return (rows_token.reshape(row_shape), rows_cotan.reshape(row_shape))


def slot_terms(rows_token, rows_cotan, weight_in, weight_down, scale_in, scale_down):
    joined = (
        jnp.einsum("rd,gdf->grf", rows_token, weight_in, preferred_element_type=jnp.float32)
        * scale_in
    )
    gate_val = joined[0]
    up_val = joined[1]
    sigmoid_val = jax.nn.sigmoid(gate_val)
    active = gate_val * sigmoid_val
    hidden = (active * up_val).astype(jnp.bfloat16)
    back_grad = (
        jnp.einsum("rd,fd->rf", rows_cotan, weight_down, preferred_element_type=jnp.float32)
        * scale_down
    )
    slope_gate = (back_grad * up_val * sigmoid_val * (1.0 + gate_val * (1.0 - sigmoid_val))).astype(
        jnp.bfloat16
    )
    slope_up = (back_grad * active).astype(jnp.bfloat16)
    slopes = jnp.stack([slope_gate, slope_up])
    grad_in = jnp.einsum("rd,grf->gdf", rows_token, slopes, preferred_element_type=jnp.float32)
    grad_down = jnp.einsum("rf,rd->fd", hidden, rows_cotan, preferred_element_type=jnp.float32)
    return (grad_in, grad_down)


def pack(part_in, part_down, groups):
    width = part_in.shape[1]
    inner = part_in.shape[2]
    return jnp.concatenate(
        [
            part_in.reshape(groups, 2 * width // groups, inner),
            part_down.reshape(groups, width // groups, inner),
        ],
        axis=1,
    )


def unpack(packed, width, inner):
    groups = packed.shape[0]
    split = 2 * width // groups
    part_in = packed[:, :split].reshape(2, width, inner)
    part_down = packed[:, split:].reshape(inner, width)
    return part_in, part_down


def exchange(block):
    return lax.all_to_all(block, "expert", 0, 0, tiled=True)


def spread_chosen(arrived, hot_experts, replica_of):
    first = lax.dynamic_index_in_dim(arrived, hot_experts[0], 0, keepdims=False)
    second = lax.dynamic_index_in_dim(arrived, hot_experts[1], 0, keepdims=False)
    wants_first = (replica_of == hot_experts[0])[:, None, None]
    outgoing = jnp.where(wants_first, first[None], second[None])
    return exchange(outgoing)


def spread_hot(packed, hot_experts, replica_of):
    return spread_chosen(exchange(packed), hot_experts, replica_of)


def body(
    slot_choices,
    mix_weights,
    tokens,
    cotangent,
    hot_experts,
    replica_of,
    weights_in,
    weights_down,
    mean_in,
    mean_down,
    square_in,
    square_down,
):
    expert_count = lax.axis_size("expert")
    tensor_count = lax.axis_size("tensor")
    token_count = slot_choices.shape[0]
    top_count = slot_choices.shape[1]
    share = (5 * token_count * top_count + 8 * expert_count * tensor_count - 1) // (
        8 * expert_count * tensor_count
    )
    capacity = share * tensor_count
    own_index = lax.axis_index("expert")
    own_in = weights_in[0]
    own_down = weights_down[0]
    width = tokens.shape[1]
    inner = own_in.shape[2]
    scale_in = 1.0 / (weight_scale * math.sqrt(width))
    scale_down = 1.0 / (weight_scale * math.sqrt(inner * tensor_count))
    own_packed = pack(own_in, own_down, expert_count)
    first_arrived = exchange(own_packed)
    token_index, present, row_weight = route_rows(
        slot_choices, mix_weights, 2 * expert_count, capacity, capacity
    )
    first_arrived, token_index, present, row_weight = lax.optimization_barrier(
        (first_arrived, token_index, present, row_weight)
    )
    held_in, held_down = unpack(
        spread_chosen(first_arrived, hot_experts, replica_of), width, inner
    )
    weight_sets = ((own_in, own_down), (held_in, held_down))
    built_token, built_cotan = gather_rows(
        token_index, present, row_weight, tokens, cotangent, 2 * expert_count, capacity
    )

    def rows_of(add_which):
        outgoing = jnp.stack([built_token[:, add_which], built_cotan[:, add_which]], axis=1)
        return exchange(outgoing)

    def terms_of(arrived_rows, add_which):
        return slot_terms(
            arrived_rows[:, 0].reshape(-1, width),
            arrived_rows[:, 1].reshape(-1, width),
            weight_sets[add_which][0],
            weight_sets[add_which][1],
            scale_in,
            scale_down,
        )

    copy_rows = rows_of(1)
    copy_in, copy_down = terms_of(copy_rows, 1)
    own_rows = rows_of(0)
    copy_packed = pack(
        (copy_in * scale_in).astype(jnp.bfloat16),
        (copy_down * scale_down).astype(jnp.bfloat16),
        expert_count,
    )
    copy_packed, own_rows = lax.optimization_barrier((copy_packed, own_rows))
    grad_in, grad_down = terms_of(own_rows, 0)
    grad_in = grad_in * scale_in
    grad_down = grad_down * scale_down
    arrived = exchange(copy_packed).astype(jnp.float32)
    sources = jnp.arange(expert_count, dtype=jnp.int32)
    sums = []
    for which in range(2):
        picked = (replica_of == hot_experts[which])[:, None, None]
        sums.append(jnp.sum(jnp.where(picked, arrived, 0.0), axis=0))
    to_owner = jnp.where(
        (sources == hot_experts[0])[:, None, None],
        sums[0][None],
        jnp.where((sources == hot_experts[1])[:, None, None], sums[1][None], 0.0),
    ).astype(jnp.bfloat16)
    gathered = exchange(to_owner).astype(jnp.float32)
    is_hot = jnp.any(hot_experts == own_index)
    own_grad = pack(grad_in, grad_down, expert_count)
    total = jnp.where(is_hot, own_grad.astype(jnp.bfloat16).astype(jnp.float32) + gathered, own_grad)
    stepped_p, averaged_p, squared_p = adam_step(
        own_packed,
        pack(mean_in[0], mean_down[0], expert_count),
        pack(square_in[0], square_down[0], expert_count),
        total,
    )
    copied_in, copied_down = unpack(spread_hot(stepped_p, hot_experts, replica_of), width, inner)
    stepped_in, stepped_down = unpack(stepped_p, width, inner)
    averaged_in, averaged_down = unpack(averaged_p, width, inner)
    squared_in, squared_down = unpack(squared_p, width, inner)
    return (
        stepped_in[None],
        stepped_down[None],
        averaged_in[None],
        averaged_down[None],
        squared_in[None],
        squared_down[None],
        copied_in[None],
        copied_down[None],
    )


def solution(mesh):
    placed = (
        P("expert", None),
        P("expert", None),
        P("expert", None),
        P("expert", None),
        P(),
        P(),
        P("expert", None, None, "tensor"),
        P("expert", "tensor", None),
        P("expert", None, None, "tensor"),
        P("expert", "tensor", None),
        P("expert", None, None, "tensor"),
        P("expert", "tensor", None),
    )
    return jax.shard_map(
        body,
        mesh=mesh,
        in_specs=placed,
        out_specs=(
            P("expert", None, None, "tensor"),
            P("expert", "tensor", None),
            P("expert", None, None, "tensor"),
            P("expert", "tensor", None),
            P("expert", None, None, "tensor"),
            P("expert", "tensor", None),
            P("expert", None, None, "tensor"),
            P("expert", "tensor", None),
        ),
        check_vma=False,
    )
```

```python
import math

import jax
import jax.numpy as jnp
from jax import lax
from jax.sharding import PartitionSpec as P

beta_one = 0.9
beta_two = 0.95
learn_rate = 0.02
decay_rate = 0.1
epsilon = 1e-08
weight_scale = 0.03


def broadcast(block, axis, source):
    block = jnp.where(lax.axis_index(axis) == source, block, jnp.zeros_like(block))
    return lax.psum(block, axis)


def adam_step(weight, moment_one, moment_two, gradient):
    first_new = beta_one * moment_one.astype(jnp.float32) + (1.0 - beta_one) * gradient
    second_new = beta_two * moment_two.astype(jnp.float32) + (1.0 - beta_two) * gradient * gradient
    base_val = weight.astype(jnp.float32)
    weight_new = base_val - learn_rate * (
        first_new / (jnp.sqrt(second_new) + epsilon) + decay_rate * base_val
    )
    return (
        weight_new.astype(jnp.bfloat16),
        first_new.astype(jnp.bfloat16),
        second_new.astype(jnp.bfloat16),
    )


def route_rows(slot_choices, mix_weights, slot_count, capacity, row_count):
    top_count = slot_choices.shape[1]
    flat_ids = slot_choices.reshape(-1)
    entries = flat_ids.shape[0]
    onehot = (flat_ids[:, None] == jnp.arange(slot_count, dtype=jnp.int32)[None, :]).astype(
        jnp.int32
    )
    before = jnp.cumsum(onehot, axis=0) - onehot
    position = jnp.sum(before * onehot, axis=1)
    target = flat_ids * capacity + position
    wanted = (
        jnp.arange(slot_count, dtype=jnp.int32)[:, None] * capacity
        + jnp.arange(row_count, dtype=jnp.int32)[None, :]
    ).reshape(-1)
    matches = wanted[:, None] == target[None, :]
    present = jnp.any(matches, axis=1)
    source = jnp.sum(jnp.where(matches, jnp.arange(entries, dtype=jnp.int32)[None, :], 0), axis=1)
    weight = jnp.where(present, mix_weights.reshape(-1)[source], 0.0)
    return source // top_count, present, weight


def gather_rows(row_index, row_scale, tokens, cotangent):
    source = jnp.concatenate([tokens, cotangent], axis=0)
    picked = source[row_index].astype(jnp.float32)
    return (row_scale[..., None] * picked).astype(jnp.bfloat16)


def order_rows(token_index, present, weight, expert_count, token_count, capacity):
    def by_kind(values):
        return jnp.swapaxes(values.reshape(expert_count, 2, capacity), 0, 1)

    lead = by_kind(token_index)
    row_index = jnp.stack([lead, lead + token_count], axis=2)
    row_scale = jnp.stack([by_kind(present.astype(jnp.float32)), by_kind(weight)], axis=2)
    return row_index, row_scale


def slot_terms(rows_token, rows_cotan, weight_in, weight_down, scale_in, scale_down):
    joined = (
        jnp.einsum("rd,gdf->grf", rows_token, weight_in, preferred_element_type=jnp.float32)
        * scale_in
    )
    gate_val = joined[0]
    up_val = joined[1]
    sigmoid_val = jax.nn.sigmoid(gate_val)
    active = gate_val * sigmoid_val
    hidden = (active * up_val).astype(jnp.bfloat16)
    back_grad = (
        jnp.einsum("rd,fd->rf", rows_cotan, weight_down, preferred_element_type=jnp.float32)
        * scale_down
    )
    slope_gate = (back_grad * up_val * sigmoid_val * (1.0 + gate_val * (1.0 - sigmoid_val))).astype(
        jnp.bfloat16
    )
    slope_up = (back_grad * active).astype(jnp.bfloat16)
    slopes = jnp.stack([slope_gate, slope_up])
    grad_in = jnp.einsum("rd,grf->gdf", rows_token, slopes, preferred_element_type=jnp.float32)
    grad_down = jnp.einsum("rf,rd->fd", hidden, rows_cotan, preferred_element_type=jnp.float32)
    return (grad_in, grad_down)


def pack(part_in, part_down, groups):
    width = part_in.shape[1]
    inner = part_in.shape[2]
    return jnp.concatenate(
        [
            part_in.reshape(groups, 2 * width // groups, inner),
            part_down.reshape(groups, width // groups, inner),
        ],
        axis=1,
    )


def unpack(packed, width, inner):
    groups = packed.shape[0]
    split = 2 * width // groups
    part_in = packed[:, :split].reshape(2, width, inner)
    part_down = packed[:, split:].reshape(inner, width)
    return part_in, part_down


def exchange(block):
    return lax.all_to_all(block, "expert", 0, 0, tiled=True)


def spread_chosen(arrived, hot_experts, replica_of):
    first = lax.dynamic_index_in_dim(arrived, hot_experts[0], 0, keepdims=False)
    second = lax.dynamic_index_in_dim(arrived, hot_experts[1], 0, keepdims=False)
    wants_first = (replica_of == hot_experts[0])[:, None, None]
    outgoing = jnp.where(wants_first, first[None], second[None])
    return exchange(outgoing)


def spread_hot(packed, hot_experts, replica_of):
    return spread_chosen(exchange(packed), hot_experts, replica_of)


def body(
    slot_choices,
    mix_weights,
    tokens,
    cotangent,
    hot_experts,
    replica_of,
    weights_in,
    weights_down,
    mean_in,
    mean_down,
    square_in,
    square_down,
):
    expert_count = lax.axis_size("expert")
    tensor_count = lax.axis_size("tensor")
    token_count = slot_choices.shape[0]
    top_count = slot_choices.shape[1]
    share = (5 * token_count * top_count + 8 * expert_count * tensor_count - 1) // (
        8 * expert_count * tensor_count
    )
    capacity = share * tensor_count
    own_index = lax.axis_index("expert")
    own_in = weights_in[0]
    own_down = weights_down[0]
    width = tokens.shape[1]
    inner = own_in.shape[2]
    scale_in = 1.0 / (weight_scale * math.sqrt(width))
    scale_down = 1.0 / (weight_scale * math.sqrt(inner * tensor_count))
    own_packed = pack(own_in, own_down, expert_count)
    first_arrived = exchange(own_packed)
    token_index, present, row_weight = route_rows(
        slot_choices, mix_weights, 2 * expert_count, capacity, capacity
    )
    row_index, row_scale = order_rows(
        token_index, present, row_weight, expert_count, tokens.shape[0], capacity
    )
    first_arrived, row_index, row_scale = lax.optimization_barrier(
        (first_arrived, row_index, row_scale)
    )
    held_in, held_down = unpack(
        spread_chosen(first_arrived, hot_experts, replica_of), width, inner
    )
    weight_sets = ((own_in, own_down), (held_in, held_down))
    built_rows = gather_rows(row_index, row_scale, tokens, cotangent)

    def rows_of(add_which):
        return exchange(built_rows[add_which])

    def terms_of(arrived_rows, add_which):
        return slot_terms(
            arrived_rows[:, 0].reshape(-1, width),
            arrived_rows[:, 1].reshape(-1, width),
            weight_sets[add_which][0],
            weight_sets[add_which][1],
            scale_in,
            scale_down,
        )

    copy_rows = rows_of(1)
    copy_in, copy_down = terms_of(copy_rows, 1)
    own_rows = rows_of(0)
    copy_packed = pack(
        (copy_in * scale_in).astype(jnp.bfloat16),
        (copy_down * scale_down).astype(jnp.bfloat16),
        expert_count,
    )
    copy_packed, own_rows = lax.optimization_barrier((copy_packed, own_rows))
    grad_in, grad_down = terms_of(own_rows, 0)
    grad_in = grad_in * scale_in
    grad_down = grad_down * scale_down
    arrived = exchange(copy_packed).astype(jnp.float32)
    sources = jnp.arange(expert_count, dtype=jnp.int32)
    sums = []
    for which in range(2):
        picked = (replica_of == hot_experts[which])[:, None, None]
        sums.append(jnp.sum(jnp.where(picked, arrived, 0.0), axis=0))
    to_owner = jnp.where(
        (sources == hot_experts[0])[:, None, None],
        sums[0][None],
        jnp.where((sources == hot_experts[1])[:, None, None], sums[1][None], 0.0),
    ).astype(jnp.bfloat16)
    gathered = exchange(to_owner).astype(jnp.float32)
    is_hot = jnp.any(hot_experts == own_index)
    own_grad = pack(grad_in, grad_down, expert_count)
    total = jnp.where(is_hot, own_grad.astype(jnp.bfloat16).astype(jnp.float32) + gathered, own_grad)
    stepped_p, averaged_p, squared_p = adam_step(
        own_packed,
        pack(mean_in[0], mean_down[0], expert_count),
        pack(square_in[0], square_down[0], expert_count),
        total,
    )
    copied_in, copied_down = unpack(spread_hot(stepped_p, hot_experts, replica_of), width, inner)
    stepped_in, stepped_down = unpack(stepped_p, width, inner)
    averaged_in, averaged_down = unpack(averaged_p, width, inner)
    squared_in, squared_down = unpack(squared_p, width, inner)
    return (
        stepped_in[None],
        stepped_down[None],
        averaged_in[None],
        averaged_down[None],
        squared_in[None],
        squared_down[None],
        copied_in[None],
        copied_down[None],
    )


def solution(mesh):
    placed = (
        P("expert", None),
        P("expert", None),
        P("expert", None),
        P("expert", None),
        P(),
        P(),
        P("expert", None, None, "tensor"),
        P("expert", "tensor", None),
        P("expert", None, None, "tensor"),
        P("expert", "tensor", None),
        P("expert", None, None, "tensor"),
        P("expert", "tensor", None),
    )
    return jax.shard_map(
        body,
        mesh=mesh,
        in_specs=placed,
        out_specs=(
            P("expert", None, None, "tensor"),
            P("expert", "tensor", None),
            P("expert", None, None, "tensor"),
            P("expert", "tensor", None),
            P("expert", None, None, "tensor"),
            P("expert", "tensor", None),
            P("expert", None, None, "tensor"),
            P("expert", "tensor", None),
        ),
        check_vma=False,
    )
```

```python
import math

import jax
import jax.numpy as jnp
from jax import lax
from jax.sharding import PartitionSpec as P

beta_one = 0.9
beta_two = 0.95
learn_rate = 0.02
decay_rate = 0.1
epsilon = 1e-08
weight_scale = 0.03


def broadcast(block, axis, source):
    block = jnp.where(lax.axis_index(axis) == source, block, jnp.zeros_like(block))
    return lax.psum(block, axis)


def adam_step(weight, moment_one, moment_two, gradient):
    first_new = beta_one * moment_one.astype(jnp.float32) + (1.0 - beta_one) * gradient
    second_new = beta_two * moment_two.astype(jnp.float32) + (1.0 - beta_two) * gradient * gradient
    base_val = weight.astype(jnp.float32)
    weight_new = base_val - learn_rate * (
        first_new / (jnp.sqrt(second_new) + epsilon) + decay_rate * base_val
    )
    return (
        weight_new.astype(jnp.bfloat16),
        first_new.astype(jnp.bfloat16),
        second_new.astype(jnp.bfloat16),
    )


def route_rows(slot_choices, mix_weights, slot_count, capacity, row_count):
    top_count = slot_choices.shape[1]
    flat_ids = slot_choices.reshape(-1)
    entries = flat_ids.shape[0]
    onehot = (flat_ids[:, None] == jnp.arange(slot_count, dtype=jnp.int32)[None, :]).astype(
        jnp.int32
    )
    before = jnp.cumsum(onehot, axis=0) - onehot
    position = jnp.sum(before * onehot, axis=1)
    target = flat_ids * capacity + position
    wanted = (
        jnp.arange(slot_count, dtype=jnp.int32)[:, None] * capacity
        + jnp.arange(row_count, dtype=jnp.int32)[None, :]
    ).reshape(-1)
    matches = wanted[:, None] == target[None, :]
    present = jnp.any(matches, axis=1)
    source = jnp.sum(jnp.where(matches, jnp.arange(entries, dtype=jnp.int32)[None, :], 0), axis=1)
    weight = jnp.where(present, mix_weights.reshape(-1)[source], 0.0)
    return source // top_count, present, weight


def gather_rows(row_index, row_scale, tokens, cotangent):
    source = jnp.concatenate([tokens, cotangent], axis=0)
    flat_index = row_index.reshape(-1)
    choose = (
        flat_index[:, None] == jnp.arange(source.shape[0], dtype=jnp.int32)[None, :]
    ).astype(source.dtype)
    picked = jnp.dot(choose, source, preferred_element_type=jnp.float32)
    scaled = row_scale.reshape(-1)[:, None] * picked
    return scaled.astype(jnp.bfloat16).reshape(row_index.shape + (source.shape[1],))


def order_rows(token_index, present, weight, expert_count, token_count, capacity):
    def by_kind(values):
        return jnp.swapaxes(values.reshape(expert_count, 2, capacity), 0, 1)

    lead = by_kind(token_index)
    row_index = jnp.stack([lead, lead + token_count], axis=2)
    row_scale = jnp.stack([by_kind(present.astype(jnp.float32)), by_kind(weight)], axis=2)
    return row_index, row_scale


def slot_terms(rows_token, rows_cotan, weight_in, weight_down, scale_in, scale_down):
    joined = (
        jnp.einsum("rd,gdf->grf", rows_token, weight_in, preferred_element_type=jnp.float32)
        * scale_in
    )
    gate_val = joined[0]
    up_val = joined[1]
    sigmoid_val = jax.nn.sigmoid(gate_val)
    active = gate_val * sigmoid_val
    hidden = (active * up_val).astype(jnp.bfloat16)
    back_grad = (
        jnp.einsum("rd,fd->rf", rows_cotan, weight_down, preferred_element_type=jnp.float32)
        * scale_down
    )
    slope_gate = (back_grad * up_val * sigmoid_val * (1.0 + gate_val * (1.0 - sigmoid_val))).astype(
        jnp.bfloat16
    )
    slope_up = (back_grad * active).astype(jnp.bfloat16)
    slopes = jnp.stack([slope_gate, slope_up])
    grad_in = jnp.einsum("rd,grf->gdf", rows_token, slopes, preferred_element_type=jnp.float32)
    grad_down = jnp.einsum("rf,rd->fd", hidden, rows_cotan, preferred_element_type=jnp.float32)
    return (grad_in, grad_down)


def pack(part_in, part_down, groups):
    width = part_in.shape[1]
    inner = part_in.shape[2]
    return jnp.concatenate(
        [
            part_in.reshape(groups, 2 * width // groups, inner),
            part_down.reshape(groups, width // groups, inner),
        ],
        axis=1,
    )


def unpack(packed, width, inner):
    groups = packed.shape[0]
    split = 2 * width // groups
    part_in = packed[:, :split].reshape(2, width, inner)
    part_down = packed[:, split:].reshape(inner, width)
    return part_in, part_down


def exchange(block):
    return lax.all_to_all(block, "expert", 0, 0, tiled=True)


def spread_chosen(arrived, hot_experts, replica_of):
    first = lax.dynamic_index_in_dim(arrived, hot_experts[0], 0, keepdims=False)
    second = lax.dynamic_index_in_dim(arrived, hot_experts[1], 0, keepdims=False)
    wants_first = (replica_of == hot_experts[0])[:, None, None]
    outgoing = jnp.where(wants_first, first[None], second[None])
    return exchange(outgoing)


def spread_hot(packed, hot_experts, replica_of):
    return spread_chosen(exchange(packed), hot_experts, replica_of)


def body(
    slot_choices,
    mix_weights,
    tokens,
    cotangent,
    hot_experts,
    replica_of,
    weights_in,
    weights_down,
    mean_in,
    mean_down,
    square_in,
    square_down,
):
    expert_count = lax.axis_size("expert")
    tensor_count = lax.axis_size("tensor")
    token_count = slot_choices.shape[0]
    top_count = slot_choices.shape[1]
    share = (5 * token_count * top_count + 8 * expert_count * tensor_count - 1) // (
        8 * expert_count * tensor_count
    )
    capacity = share * tensor_count
    own_index = lax.axis_index("expert")
    own_in = weights_in[0]
    own_down = weights_down[0]
    width = tokens.shape[1]
    inner = own_in.shape[2]
    scale_in = 1.0 / (weight_scale * math.sqrt(width))
    scale_down = 1.0 / (weight_scale * math.sqrt(inner * tensor_count))
    own_packed = pack(own_in, own_down, expert_count)
    first_arrived = exchange(own_packed)
    token_index, present, row_weight = route_rows(
        slot_choices, mix_weights, 2 * expert_count, capacity, capacity
    )
    row_index, row_scale = order_rows(
        token_index, present, row_weight, expert_count, tokens.shape[0], capacity
    )
    first_arrived, row_index, row_scale = lax.optimization_barrier(
        (first_arrived, row_index, row_scale)
    )
    held_packed = spread_chosen(first_arrived, hot_experts, replica_of)
    built_rows = gather_rows(row_index, row_scale, tokens, cotangent)

    def rows_of(add_which):
        return exchange(built_rows[add_which])

    copy_rows = rows_of(1)
    copy_rows, held_packed = lax.optimization_barrier((copy_rows, held_packed))
    held_in, held_down = unpack(held_packed, width, inner)
    weight_sets = ((own_in, own_down), (held_in, held_down))

    def terms_of(arrived_rows, add_which):
        return slot_terms(
            arrived_rows[:, 0].reshape(-1, width),
            arrived_rows[:, 1].reshape(-1, width),
            weight_sets[add_which][0],
            weight_sets[add_which][1],
            scale_in,
            scale_down,
        )

    copy_in, copy_down = terms_of(copy_rows, 1)
    own_rows = rows_of(0)
    copy_packed = pack(
        (copy_in * scale_in).astype(jnp.bfloat16),
        (copy_down * scale_down).astype(jnp.bfloat16),
        expert_count,
    )
    copy_packed, own_rows = lax.optimization_barrier((copy_packed, own_rows))
    grad_in, grad_down = terms_of(own_rows, 0)
    grad_in = grad_in * scale_in
    grad_down = grad_down * scale_down
    arrived = exchange(copy_packed).astype(jnp.float32)
    sources = jnp.arange(expert_count, dtype=jnp.int32)
    sums = []
    for which in range(2):
        picked = (replica_of == hot_experts[which])[:, None, None]
        sums.append(jnp.sum(jnp.where(picked, arrived, 0.0), axis=0))
    to_owner = jnp.where(
        (sources == hot_experts[0])[:, None, None],
        sums[0][None],
        jnp.where((sources == hot_experts[1])[:, None, None], sums[1][None], 0.0),
    ).astype(jnp.bfloat16)
    gathered = exchange(to_owner).astype(jnp.float32)
    is_hot = jnp.any(hot_experts == own_index)
    own_grad = pack(grad_in, grad_down, expert_count)
    total = jnp.where(is_hot, own_grad.astype(jnp.bfloat16).astype(jnp.float32) + gathered, own_grad)
    stepped_p, averaged_p, squared_p = adam_step(
        own_packed,
        pack(mean_in[0], mean_down[0], expert_count),
        pack(square_in[0], square_down[0], expert_count),
        total,
    )
    copied_in, copied_down = unpack(spread_hot(stepped_p, hot_experts, replica_of), width, inner)
    stepped_in, stepped_down = unpack(stepped_p, width, inner)
    averaged_in, averaged_down = unpack(averaged_p, width, inner)
    squared_in, squared_down = unpack(squared_p, width, inner)
    return (
        stepped_in[None],
        stepped_down[None],
        averaged_in[None],
        averaged_down[None],
        squared_in[None],
        squared_down[None],
        copied_in[None],
        copied_down[None],
    )


def solution(mesh):
    placed = (
        P("expert", None),
        P("expert", None),
        P("expert", None),
        P("expert", None),
        P(),
        P(),
        P("expert", None, None, "tensor"),
        P("expert", "tensor", None),
        P("expert", None, None, "tensor"),
        P("expert", "tensor", None),
        P("expert", None, None, "tensor"),
        P("expert", "tensor", None),
    )
    return jax.shard_map(
        body,
        mesh=mesh,
        in_specs=placed,
        out_specs=(
            P("expert", None, None, "tensor"),
            P("expert", "tensor", None),
            P("expert", None, None, "tensor"),
            P("expert", "tensor", None),
            P("expert", None, None, "tensor"),
            P("expert", "tensor", None),
            P("expert", None, None, "tensor"),
            P("expert", "tensor", None),
        ),
        check_vma=False,
    )
```

```python
import math

import jax
import jax.numpy as jnp
from jax import lax
from jax.sharding import PartitionSpec as P

beta_one = 0.9
beta_two = 0.95
learn_rate = 0.02
decay_rate = 0.1
epsilon = 1e-08
weight_scale = 0.03


def broadcast(block, axis, source):
    block = jnp.where(lax.axis_index(axis) == source, block, jnp.zeros_like(block))
    return lax.psum(block, axis)


def adam_step(weight, moment_one, moment_two, gradient):
    first_new = beta_one * moment_one.astype(jnp.float32) + (1.0 - beta_one) * gradient
    second_new = beta_two * moment_two.astype(jnp.float32) + (1.0 - beta_two) * gradient * gradient
    base_val = weight.astype(jnp.float32)
    weight_new = base_val - learn_rate * (
        first_new / (jnp.sqrt(second_new) + epsilon) + decay_rate * base_val
    )
    return (
        weight_new.astype(jnp.bfloat16),
        first_new.astype(jnp.bfloat16),
        second_new.astype(jnp.bfloat16),
    )


def route_rows(slot_choices, mix_weights, slot_count, capacity, row_count):
    top_count = slot_choices.shape[1]
    flat_ids = slot_choices.reshape(-1)
    entries = flat_ids.shape[0]
    onehot = (flat_ids[:, None] == jnp.arange(slot_count, dtype=jnp.int32)[None, :]).astype(
        jnp.int32
    )
    before = jnp.cumsum(onehot, axis=0) - onehot
    position = jnp.sum(before * onehot, axis=1)
    target = flat_ids * capacity + position
    wanted = (
        jnp.arange(slot_count, dtype=jnp.int32)[:, None] * capacity
        + jnp.arange(row_count, dtype=jnp.int32)[None, :]
    ).reshape(-1)
    matches = wanted[:, None] == target[None, :]
    present = jnp.any(matches, axis=1)
    source = jnp.sum(jnp.where(matches, jnp.arange(entries, dtype=jnp.int32)[None, :], 0), axis=1)
    weight = jnp.where(present, mix_weights.reshape(-1)[source], 0.0)
    return source // top_count, present, weight


def gather_rows(row_index, row_scale, tokens, cotangent):
    source = jnp.concatenate([tokens, cotangent], axis=0)
    flat_index = row_index.reshape(-1)
    choose = (
        flat_index[:, None] == jnp.arange(source.shape[0], dtype=jnp.int32)[None, :]
    ).astype(source.dtype)
    picked = jnp.dot(choose, source, preferred_element_type=jnp.float32)
    scaled = row_scale.reshape(-1)[:, None] * picked
    return scaled.astype(jnp.bfloat16).reshape(row_index.shape + (source.shape[1],))


def order_rows(token_index, present, weight, expert_count, token_count, capacity):
    def by_kind(values):
        return jnp.swapaxes(values.reshape(expert_count, 2, capacity), 0, 1)

    lead = by_kind(token_index)
    row_index = jnp.stack([lead, lead + token_count], axis=2)
    row_scale = jnp.stack([by_kind(present.astype(jnp.float32)), by_kind(weight)], axis=2)
    return row_index, row_scale


def slot_terms(rows_token, rows_cotan, weight_in, weight_down, scale_in, scale_down):
    joined = (
        jnp.einsum("rd,gdf->grf", rows_token, weight_in, preferred_element_type=jnp.float32)
        * scale_in
    )
    gate_val = joined[0]
    up_val = joined[1]
    sigmoid_val = jax.nn.sigmoid(gate_val)
    active = gate_val * sigmoid_val
    hidden = (active * up_val).astype(jnp.bfloat16)
    back_grad = (
        jnp.einsum("rd,fd->rf", rows_cotan, weight_down, preferred_element_type=jnp.float32)
        * scale_down
    )
    slope_gate = (back_grad * up_val * sigmoid_val * (1.0 + gate_val * (1.0 - sigmoid_val))).astype(
        jnp.bfloat16
    )
    slope_up = (back_grad * active).astype(jnp.bfloat16)
    slopes = jnp.stack([slope_gate, slope_up])
    grad_in = jnp.einsum("rd,grf->gdf", rows_token, slopes, preferred_element_type=jnp.float32)
    grad_down = jnp.einsum("rf,rd->fd", hidden, rows_cotan, preferred_element_type=jnp.float32)
    return (grad_in, grad_down)


def pack(part_in, part_down, groups):
    width = part_in.shape[1]
    inner = part_in.shape[2]
    return jnp.concatenate(
        [
            part_in.reshape(groups, 2 * width // groups, inner),
            part_down.reshape(groups, width // groups, inner),
        ],
        axis=1,
    )


def unpack(packed, width, inner):
    groups = packed.shape[0]
    split = 2 * width // groups
    part_in = packed[:, :split].reshape(2, width, inner)
    part_down = packed[:, split:].reshape(inner, width)
    return part_in, part_down


def exchange(block):
    return lax.all_to_all(block, "expert", 0, 0, tiled=True)


def spread_chosen(arrived, hot_experts, replica_of):
    first = lax.dynamic_index_in_dim(arrived, hot_experts[0], 0, keepdims=False)
    second = lax.dynamic_index_in_dim(arrived, hot_experts[1], 0, keepdims=False)
    wants_first = (replica_of == hot_experts[0])[:, None, None]
    outgoing = jnp.where(wants_first, first[None], second[None])
    return exchange(outgoing)


def spread_hot(packed, hot_experts, replica_of):
    return spread_chosen(exchange(packed), hot_experts, replica_of)


def body(
    slot_choices,
    mix_weights,
    tokens,
    cotangent,
    hot_experts,
    replica_of,
    weights_in,
    weights_down,
    mean_in,
    mean_down,
    square_in,
    square_down,
):
    expert_count = lax.axis_size("expert")
    tensor_count = lax.axis_size("tensor")
    token_count = slot_choices.shape[0]
    top_count = slot_choices.shape[1]
    share = (5 * token_count * top_count + 8 * expert_count * tensor_count - 1) // (
        8 * expert_count * tensor_count
    )
    capacity = share * tensor_count
    own_index = lax.axis_index("expert")
    own_in = weights_in[0]
    own_down = weights_down[0]
    width = tokens.shape[1]
    inner = own_in.shape[2]
    scale_in = 1.0 / (weight_scale * math.sqrt(width))
    scale_down = 1.0 / (weight_scale * math.sqrt(inner * tensor_count))
    own_packed = pack(own_in, own_down, expert_count)
    first_arrived = exchange(own_packed)
    token_index, present, row_weight = route_rows(
        slot_choices, mix_weights, 2 * expert_count, capacity, capacity
    )
    row_index, row_scale = order_rows(
        token_index, present, row_weight, expert_count, tokens.shape[0], capacity
    )
    first_arrived, row_index, row_scale = lax.optimization_barrier(
        (first_arrived, row_index, row_scale)
    )
    both_hot = jnp.stack(
        [
            lax.dynamic_index_in_dim(first_arrived, hot_experts[which], 0, keepdims=False)
            for which in range(2)
        ]
    )
    every_chunk = lax.all_gather(both_hot, "expert", axis=0)
    wanted_hot = (replica_of[own_index] == hot_experts[1]).astype(jnp.int32)
    held_packed = lax.dynamic_index_in_dim(every_chunk, wanted_hot, 1, keepdims=False)
    built_rows = gather_rows(row_index, row_scale, tokens, cotangent)

    def rows_of(add_which):
        return exchange(built_rows[add_which])

    copy_rows = rows_of(1)
    copy_rows, held_packed = lax.optimization_barrier((copy_rows, held_packed))
    held_in, held_down = unpack(held_packed, width, inner)
    weight_sets = ((own_in, own_down), (held_in, held_down))

    def terms_of(arrived_rows, add_which):
        return slot_terms(
            arrived_rows[:, 0].reshape(-1, width),
            arrived_rows[:, 1].reshape(-1, width),
            weight_sets[add_which][0],
            weight_sets[add_which][1],
            scale_in,
            scale_down,
        )

    copy_in, copy_down = terms_of(copy_rows, 1)
    own_rows = rows_of(0)
    copy_packed = pack(
        (copy_in * scale_in).astype(jnp.bfloat16),
        (copy_down * scale_down).astype(jnp.bfloat16),
        expert_count,
    )
    copy_packed, own_rows = lax.optimization_barrier((copy_packed, own_rows))
    grad_in, grad_down = terms_of(own_rows, 0)
    grad_in = grad_in * scale_in
    grad_down = grad_down * scale_down
    arrived = exchange(copy_packed).astype(jnp.float32)
    sources = jnp.arange(expert_count, dtype=jnp.int32)
    sums = []
    for which in range(2):
        picked = (replica_of == hot_experts[which])[:, None, None]
        sums.append(jnp.sum(jnp.where(picked, arrived, 0.0), axis=0))
    to_owner = jnp.where(
        (sources == hot_experts[0])[:, None, None],
        sums[0][None],
        jnp.where((sources == hot_experts[1])[:, None, None], sums[1][None], 0.0),
    ).astype(jnp.bfloat16)
    gathered = exchange(to_owner).astype(jnp.float32)
    is_hot = jnp.any(hot_experts == own_index)
    own_grad = pack(grad_in, grad_down, expert_count)
    total = jnp.where(is_hot, own_grad.astype(jnp.bfloat16).astype(jnp.float32) + gathered, own_grad)
    stepped_p, averaged_p, squared_p = adam_step(
        own_packed,
        pack(mean_in[0], mean_down[0], expert_count),
        pack(square_in[0], square_down[0], expert_count),
        total,
    )
    copied_in, copied_down = unpack(spread_hot(stepped_p, hot_experts, replica_of), width, inner)
    stepped_in, stepped_down = unpack(stepped_p, width, inner)
    averaged_in, averaged_down = unpack(averaged_p, width, inner)
    squared_in, squared_down = unpack(squared_p, width, inner)
    return (
        stepped_in[None],
        stepped_down[None],
        averaged_in[None],
        averaged_down[None],
        squared_in[None],
        squared_down[None],
        copied_in[None],
        copied_down[None],
    )


def solution(mesh):
    placed = (
        P("expert", None),
        P("expert", None),
        P("expert", None),
        P("expert", None),
        P(),
        P(),
        P("expert", None, None, "tensor"),
        P("expert", "tensor", None),
        P("expert", None, None, "tensor"),
        P("expert", "tensor", None),
        P("expert", None, None, "tensor"),
        P("expert", "tensor", None),
    )
    return jax.shard_map(
        body,
        mesh=mesh,
        in_specs=placed,
        out_specs=(
            P("expert", None, None, "tensor"),
            P("expert", "tensor", None),
            P("expert", None, None, "tensor"),
            P("expert", "tensor", None),
            P("expert", None, None, "tensor"),
            P("expert", "tensor", None),
            P("expert", None, None, "tensor"),
            P("expert", "tensor", None),
        ),
        check_vma=False,
    )
```

```python
import math

import jax
import jax.numpy as jnp
from jax import lax
from jax.sharding import PartitionSpec as P

beta_one = 0.9
beta_two = 0.95
learn_rate = 0.02
decay_rate = 0.1
epsilon = 1e-08
weight_scale = 0.03


def broadcast(block, axis, source):
    block = jnp.where(lax.axis_index(axis) == source, block, jnp.zeros_like(block))
    return lax.psum(block, axis)


def adam_step(weight, moment_one, moment_two, gradient):
    first_new = beta_one * moment_one.astype(jnp.float32) + (1.0 - beta_one) * gradient
    second_new = beta_two * moment_two.astype(jnp.float32) + (1.0 - beta_two) * gradient * gradient
    base_val = weight.astype(jnp.float32)
    weight_new = base_val - learn_rate * (
        first_new / (jnp.sqrt(second_new) + epsilon) + decay_rate * base_val
    )
    return (
        weight_new.astype(jnp.bfloat16),
        first_new.astype(jnp.bfloat16),
        second_new.astype(jnp.bfloat16),
    )


def route_rows(slot_choices, mix_weights, slot_count, capacity, row_count):
    top_count = slot_choices.shape[1]
    flat_ids = slot_choices.reshape(-1)
    entries = flat_ids.shape[0]
    onehot = (flat_ids[:, None] == jnp.arange(slot_count, dtype=jnp.int32)[None, :]).astype(
        jnp.int32
    )
    before = jnp.cumsum(onehot, axis=0) - onehot
    position = jnp.sum(before * onehot, axis=1)
    target = flat_ids * capacity + position
    wanted = (
        jnp.arange(slot_count, dtype=jnp.int32)[:, None] * capacity
        + jnp.arange(row_count, dtype=jnp.int32)[None, :]
    ).reshape(-1)
    matches = wanted[:, None] == target[None, :]
    present = jnp.any(matches, axis=1)
    source = jnp.sum(jnp.where(matches, jnp.arange(entries, dtype=jnp.int32)[None, :], 0), axis=1)
    weight = jnp.where(present, mix_weights.reshape(-1)[source], 0.0)
    return source // top_count, present, weight


def gather_rows(row_index, row_scale, tokens, cotangent):
    source = jnp.concatenate([tokens, cotangent], axis=0)
    flat_index = row_index.reshape(-1)
    choose = (
        flat_index[:, None] == jnp.arange(source.shape[0], dtype=jnp.int32)[None, :]
    ).astype(source.dtype)
    picked = jnp.dot(choose, source, preferred_element_type=jnp.float32)
    scaled = row_scale.reshape(-1)[:, None] * picked
    return scaled.astype(jnp.bfloat16).reshape(row_index.shape + (source.shape[1],))


def order_rows(token_index, present, weight, expert_count, token_count, capacity):
    def by_kind(values):
        return jnp.swapaxes(values.reshape(expert_count, 2, capacity), 0, 1)

    lead = by_kind(token_index)
    row_index = jnp.stack([lead, lead + token_count], axis=2)
    row_scale = jnp.stack([by_kind(present.astype(jnp.float32)), by_kind(weight)], axis=2)
    return row_index, row_scale


def slot_terms(rows_token, rows_cotan, weight_in, weight_down_t, scale_in, scale_down):
    joined = (
        jnp.einsum("rd,gdf->grf", rows_token, weight_in, preferred_element_type=jnp.float32)
        * scale_in
    )
    gate_val = joined[0]
    up_val = joined[1]
    sigmoid_val = jax.nn.sigmoid(gate_val)
    active = gate_val * sigmoid_val
    hidden = (active * up_val).astype(jnp.bfloat16)
    back_grad = (
        jnp.einsum("rd,df->rf", rows_cotan, weight_down_t, preferred_element_type=jnp.float32)
        * scale_down
    )
    slope_gate = (back_grad * up_val * sigmoid_val * (1.0 + gate_val * (1.0 - sigmoid_val))).astype(
        jnp.bfloat16
    )
    slope_up = (back_grad * active).astype(jnp.bfloat16)
    slopes = jnp.stack([slope_gate, slope_up])
    grad_in = jnp.einsum("rd,grf->gdf", rows_token, slopes, preferred_element_type=jnp.float32)
    grad_down_t = jnp.einsum("rf,rd->df", hidden, rows_cotan, preferred_element_type=jnp.float32)
    return (grad_in, grad_down_t)


def pack(part_in, part_down, groups):
    return pack_t(part_in, part_down.T, groups)


def pack_t(part_in, part_down_t, groups):
    width = part_in.shape[1]
    inner = part_in.shape[2]
    return jnp.concatenate(
        [
            part_in.reshape(groups, 2 * width // groups, inner),
            part_down_t.reshape(groups, width // groups, inner),
        ],
        axis=1,
    )


def unpack_t(packed, width, inner):
    groups = packed.shape[0]
    split = 2 * width // groups
    part_in = packed[:, :split].reshape(2, width, inner)
    part_down_t = packed[:, split:].reshape(width, inner)
    return part_in, part_down_t


def unpack(packed, width, inner):
    part_in, part_down_t = unpack_t(packed, width, inner)
    return part_in, part_down_t.T


def exchange(block):
    return lax.all_to_all(block, "expert", 0, 0, tiled=True)


def spread_chosen(arrived, hot_experts, replica_of):
    first = lax.dynamic_index_in_dim(arrived, hot_experts[0], 0, keepdims=False)
    second = lax.dynamic_index_in_dim(arrived, hot_experts[1], 0, keepdims=False)
    wants_first = (replica_of == hot_experts[0])[:, None, None]
    outgoing = jnp.where(wants_first, first[None], second[None])
    return exchange(outgoing)


def spread_hot(packed, hot_experts, replica_of):
    return spread_chosen(exchange(packed), hot_experts, replica_of)


def body(
    slot_choices,
    mix_weights,
    tokens,
    cotangent,
    hot_experts,
    replica_of,
    weights_in,
    weights_down,
    mean_in,
    mean_down,
    square_in,
    square_down,
):
    expert_count = lax.axis_size("expert")
    tensor_count = lax.axis_size("tensor")
    token_count = slot_choices.shape[0]
    top_count = slot_choices.shape[1]
    share = (5 * token_count * top_count + 8 * expert_count * tensor_count - 1) // (
        8 * expert_count * tensor_count
    )
    capacity = share * tensor_count
    own_index = lax.axis_index("expert")
    own_in = weights_in[0]
    own_down = weights_down[0]
    width = tokens.shape[1]
    inner = own_in.shape[2]
    scale_in = 1.0 / (weight_scale * math.sqrt(width))
    scale_down = 1.0 / (weight_scale * math.sqrt(inner * tensor_count))
    own_packed = pack(own_in, own_down, expert_count)
    first_arrived = exchange(own_packed)
    token_index, present, row_weight = route_rows(
        slot_choices, mix_weights, 2 * expert_count, capacity, capacity
    )
    row_index, row_scale = order_rows(
        token_index, present, row_weight, expert_count, tokens.shape[0], capacity
    )
    first_arrived, row_index, row_scale = lax.optimization_barrier(
        (first_arrived, row_index, row_scale)
    )
    held_packed = spread_chosen(first_arrived, hot_experts, replica_of)
    built_rows = gather_rows(row_index, row_scale, tokens, cotangent)

    def rows_of(add_which):
        return exchange(built_rows[add_which])

    copy_rows = rows_of(1)
    copy_rows, held_packed = lax.optimization_barrier((copy_rows, held_packed))
    held_in, held_down_t = unpack_t(held_packed, width, inner)
    weight_sets = ((own_in, own_down.T), (held_in, held_down_t))

    def terms_of(arrived_rows, add_which):
        return slot_terms(
            arrived_rows[:, 0].reshape(-1, width),
            arrived_rows[:, 1].reshape(-1, width),
            weight_sets[add_which][0],
            weight_sets[add_which][1],
            scale_in,
            scale_down,
        )

    copy_in, copy_down = terms_of(copy_rows, 1)
    own_rows = rows_of(0)
    copy_packed = pack_t(
        (copy_in * scale_in).astype(jnp.bfloat16),
        (copy_down * scale_down).astype(jnp.bfloat16),
        expert_count,
    )
    copy_packed, own_rows = lax.optimization_barrier((copy_packed, own_rows))
    grad_in, grad_down = terms_of(own_rows, 0)
    grad_in = grad_in * scale_in
    grad_down = grad_down * scale_down
    arrived = exchange(copy_packed).astype(jnp.float32)
    sources = jnp.arange(expert_count, dtype=jnp.int32)
    sums = []
    for which in range(2):
        picked = (replica_of == hot_experts[which])[:, None, None]
        sums.append(jnp.sum(jnp.where(picked, arrived, 0.0), axis=0))
    to_owner = jnp.where(
        (sources == hot_experts[0])[:, None, None],
        sums[0][None],
        jnp.where((sources == hot_experts[1])[:, None, None], sums[1][None], 0.0),
    ).astype(jnp.bfloat16)
    gathered = exchange(to_owner).astype(jnp.float32)
    is_hot = jnp.any(hot_experts == own_index)
    own_grad = pack_t(grad_in, grad_down, expert_count)
    total = jnp.where(is_hot, own_grad.astype(jnp.bfloat16).astype(jnp.float32) + gathered, own_grad)
    stepped_p, averaged_p, squared_p = adam_step(
        own_packed,
        pack(mean_in[0], mean_down[0], expert_count),
        pack(square_in[0], square_down[0], expert_count),
        total,
    )
    copied_in, copied_down = unpack(spread_hot(stepped_p, hot_experts, replica_of), width, inner)
    stepped_in, stepped_down = unpack(stepped_p, width, inner)
    averaged_in, averaged_down = unpack(averaged_p, width, inner)
    squared_in, squared_down = unpack(squared_p, width, inner)
    return (
        stepped_in[None],
        stepped_down[None],
        averaged_in[None],
        averaged_down[None],
        squared_in[None],
        squared_down[None],
        copied_in[None],
        copied_down[None],
    )


def solution(mesh):
    placed = (
        P("expert", None),
        P("expert", None),
        P("expert", None),
        P("expert", None),
        P(),
        P(),
        P("expert", None, None, "tensor"),
        P("expert", "tensor", None),
        P("expert", None, None, "tensor"),
        P("expert", "tensor", None),
        P("expert", None, None, "tensor"),
        P("expert", "tensor", None),
    )
    return jax.shard_map(
        body,
        mesh=mesh,
        in_specs=placed,
        out_specs=(
            P("expert", None, None, "tensor"),
            P("expert", "tensor", None),
            P("expert", None, None, "tensor"),
            P("expert", "tensor", None),
            P("expert", None, None, "tensor"),
            P("expert", "tensor", None),
            P("expert", None, None, "tensor"),
            P("expert", "tensor", None),
        ),
        check_vma=False,
    )
```

```python
import math

import jax
import jax.numpy as jnp
from jax import lax
from jax.sharding import PartitionSpec as P

beta_one = 0.9
beta_two = 0.95
learn_rate = 0.02
decay_rate = 0.1
epsilon = 1e-08
weight_scale = 0.03


def broadcast(block, axis, source):
    block = jnp.where(lax.axis_index(axis) == source, block, jnp.zeros_like(block))
    return lax.psum(block, axis)


def adam_step(weight, moment_one, moment_two, gradient):
    first_new = beta_one * moment_one.astype(jnp.float32) + (1.0 - beta_one) * gradient
    second_new = beta_two * moment_two.astype(jnp.float32) + (1.0 - beta_two) * gradient * gradient
    base_val = weight.astype(jnp.float32)
    weight_new = base_val - learn_rate * (
        first_new / (jnp.sqrt(second_new) + epsilon) + decay_rate * base_val
    )
    return (
        weight_new.astype(jnp.bfloat16),
        first_new.astype(jnp.bfloat16),
        second_new.astype(jnp.bfloat16),
    )


def route_rows(slot_choices, mix_weights, slot_count, capacity, row_count):
    top_count = slot_choices.shape[1]
    flat_ids = slot_choices.reshape(-1)
    entries = flat_ids.shape[0]
    onehot = (flat_ids[:, None] == jnp.arange(slot_count, dtype=jnp.int32)[None, :]).astype(
        jnp.int32
    )
    before = jnp.cumsum(onehot, axis=0) - onehot
    position = jnp.sum(before * onehot, axis=1)
    target = flat_ids * capacity + position
    wanted = (
        jnp.arange(slot_count, dtype=jnp.int32)[:, None] * capacity
        + jnp.arange(row_count, dtype=jnp.int32)[None, :]
    ).reshape(-1)
    matches = wanted[:, None] == target[None, :]
    present = jnp.any(matches, axis=1)
    source = jnp.sum(jnp.where(matches, jnp.arange(entries, dtype=jnp.int32)[None, :], 0), axis=1)
    weight = jnp.where(present, mix_weights.reshape(-1)[source], 0.0)
    return source // top_count, present, weight


def gather_rows(row_index, row_scale, tokens, cotangent):
    source = jnp.concatenate([tokens, cotangent], axis=0)
    flat_index = row_index.reshape(-1)
    choose = (
        flat_index[:, None] == jnp.arange(source.shape[0], dtype=jnp.int32)[None, :]
    ).astype(source.dtype)
    picked = jnp.dot(choose, source, preferred_element_type=jnp.float32)
    scaled = row_scale.reshape(-1)[:, None] * picked
    return scaled.astype(jnp.bfloat16).reshape(row_index.shape + (source.shape[1],))


def order_rows(token_index, present, weight, expert_count, token_count, capacity):
    def by_kind(values):
        return jnp.swapaxes(values.reshape(expert_count, 2, capacity), 0, 1)

    lead = by_kind(token_index)
    row_index = jnp.stack([lead, lead + token_count], axis=2)
    row_scale = jnp.stack([by_kind(present.astype(jnp.float32)), by_kind(weight)], axis=2)
    return row_index, row_scale


def slot_terms(rows_token, rows_cotan, weight_in, weight_down_t, scale_in, scale_down):
    joined = (
        jnp.einsum("rd,gdf->grf", rows_token, weight_in, preferred_element_type=jnp.float32)
        * scale_in
    )
    gate_val = joined[0]
    up_val = joined[1]
    sigmoid_val = jax.nn.sigmoid(gate_val)
    active = gate_val * sigmoid_val
    hidden = (active * up_val).astype(jnp.bfloat16)
    back_grad = (
        jnp.einsum("rd,df->rf", rows_cotan, weight_down_t, preferred_element_type=jnp.float32)
        * scale_down
    )
    slope_gate = (back_grad * up_val * sigmoid_val * (1.0 + gate_val * (1.0 - sigmoid_val))).astype(
        jnp.bfloat16
    )
    slope_up = (back_grad * active).astype(jnp.bfloat16)
    slopes = jnp.stack([slope_gate, slope_up])
    grad_in = jnp.einsum("rd,grf->gdf", rows_token, slopes, preferred_element_type=jnp.float32)
    grad_down_t = jnp.einsum("rf,rd->df", hidden, rows_cotan, preferred_element_type=jnp.float32)
    return (grad_in, grad_down_t)


def pack(part_in, part_down, groups):
    return pack_t(part_in, part_down.T, groups)


def pack_t(part_in, part_down_t, groups):
    width = part_in.shape[1]
    inner = part_in.shape[2]
    return jnp.concatenate(
        [
            part_in.reshape(groups, 2 * width // groups, inner),
            part_down_t.reshape(groups, width // groups, inner),
        ],
        axis=1,
    )


def unpack_t(packed, width, inner):
    groups = packed.shape[0]
    split = 2 * width // groups
    part_in = packed[:, :split].reshape(2, width, inner)
    part_down_t = packed[:, split:].reshape(width, inner)
    return part_in, part_down_t


def unpack(packed, width, inner):
    part_in, part_down_t = unpack_t(packed, width, inner)
    return part_in, part_down_t.T


def exchange(block):
    return lax.all_to_all(block, "expert", 0, 0, tiled=True)


def spread_chosen(arrived, hot_experts, replica_of):
    first = lax.dynamic_index_in_dim(arrived, hot_experts[0], 0, keepdims=False)
    second = lax.dynamic_index_in_dim(arrived, hot_experts[1], 0, keepdims=False)
    wants_first = (replica_of == hot_experts[0])[:, None, None]
    outgoing = jnp.where(wants_first, first[None], second[None])
    return exchange(outgoing)


def spread_hot(packed, hot_experts, replica_of):
    return spread_chosen(exchange(packed), hot_experts, replica_of)


def body(
    slot_choices,
    mix_weights,
    tokens,
    cotangent,
    hot_experts,
    replica_of,
    weights_in,
    weights_down,
    mean_in,
    mean_down,
    square_in,
    square_down,
):
    expert_count = lax.axis_size("expert")
    tensor_count = lax.axis_size("tensor")
    token_count = slot_choices.shape[0]
    top_count = slot_choices.shape[1]
    share = (5 * token_count * top_count + 8 * expert_count * tensor_count - 1) // (
        8 * expert_count * tensor_count
    )
    capacity = share * tensor_count
    own_index = lax.axis_index("expert")
    own_in = weights_in[0]
    own_down = weights_down[0]
    width = tokens.shape[1]
    inner = own_in.shape[2]
    scale_in = 1.0 / (weight_scale * math.sqrt(width))
    scale_down = 1.0 / (weight_scale * math.sqrt(inner * tensor_count))
    own_packed = pack(own_in, own_down, expert_count)
    first_arrived = exchange(own_packed)
    token_index, present, row_weight = route_rows(
        slot_choices, mix_weights, 2 * expert_count, capacity, capacity
    )
    row_index, row_scale = order_rows(
        token_index, present, row_weight, expert_count, tokens.shape[0], capacity
    )
    first_arrived, row_index, row_scale = lax.optimization_barrier(
        (first_arrived, row_index, row_scale)
    )
    held_packed = spread_chosen(first_arrived, hot_experts, replica_of)
    built_rows = gather_rows(row_index, row_scale, tokens, cotangent)

    def rows_of(add_which):
        return exchange(built_rows[add_which])

    copy_rows = rows_of(1)
    copy_rows, held_packed = lax.optimization_barrier((copy_rows, held_packed))
    held_in, held_down_t = unpack_t(held_packed, width, inner)
    weight_sets = ((own_in, own_down.T), (held_in, held_down_t))

    def terms_of(arrived_rows, add_which):
        return slot_terms(
            arrived_rows[:, 0].reshape(-1, width),
            arrived_rows[:, 1].reshape(-1, width),
            weight_sets[add_which][0],
            weight_sets[add_which][1],
            scale_in,
            scale_down,
        )

    copy_in, copy_down = terms_of(copy_rows, 1)
    own_rows = rows_of(0)
    copy_packed = pack_t(
        (copy_in * scale_in).astype(jnp.bfloat16),
        (copy_down * scale_down).astype(jnp.bfloat16),
        expert_count,
    )
    copy_packed, own_rows = lax.optimization_barrier((copy_packed, own_rows))
    grad_in, grad_down = terms_of(own_rows, 0)
    grad_in = grad_in * scale_in
    grad_down = grad_down * scale_down
    arrived = exchange(copy_packed).astype(jnp.float32)
    sources = jnp.arange(expert_count, dtype=jnp.int32)
    sums = []
    for which in range(2):
        picked = (replica_of == hot_experts[which])[:, None, None]
        sums.append(jnp.sum(jnp.where(picked, arrived, 0.0), axis=0))
    to_owner = jnp.where(
        (sources == hot_experts[0])[:, None, None],
        sums[0][None],
        jnp.where((sources == hot_experts[1])[:, None, None], sums[1][None], 0.0),
    ).astype(jnp.bfloat16)
    gathered_low = exchange(to_owner)
    is_hot = jnp.any(hot_experts == own_index)

    def adam_of(gathered_low, grad_in, grad_down):
        own_grad = pack_t(grad_in, grad_down, expert_count)
        total = jnp.where(
            is_hot,
            own_grad.astype(jnp.bfloat16).astype(jnp.float32) + gathered_low.astype(jnp.float32),
            own_grad,
        )
        return adam_step(
            own_packed,
            pack(mean_in[0], mean_down[0], expert_count),
            pack(square_in[0], square_down[0], expert_count),
            total,
        )

    stepped_p = adam_of(gathered_low, grad_in, grad_down)[0]
    stepped_p, gathered_low, grad_in, grad_down = lax.optimization_barrier(
        (stepped_p, gathered_low, grad_in, grad_down)
    )
    _, averaged_p, squared_p = adam_of(gathered_low, grad_in, grad_down)
    copied_in, copied_down = unpack(spread_hot(stepped_p, hot_experts, replica_of), width, inner)
    stepped_in, stepped_down = unpack(stepped_p, width, inner)
    averaged_in, averaged_down = unpack(averaged_p, width, inner)
    squared_in, squared_down = unpack(squared_p, width, inner)
    return (
        stepped_in[None],
        stepped_down[None],
        averaged_in[None],
        averaged_down[None],
        squared_in[None],
        squared_down[None],
        copied_in[None],
        copied_down[None],
    )


def solution(mesh):
    placed = (
        P("expert", None),
        P("expert", None),
        P("expert", None),
        P("expert", None),
        P(),
        P(),
        P("expert", None, None, "tensor"),
        P("expert", "tensor", None),
        P("expert", None, None, "tensor"),
        P("expert", "tensor", None),
        P("expert", None, None, "tensor"),
        P("expert", "tensor", None),
    )
    return jax.shard_map(
        body,
        mesh=mesh,
        in_specs=placed,
        out_specs=(
            P("expert", None, None, "tensor"),
            P("expert", "tensor", None),
            P("expert", None, None, "tensor"),
            P("expert", "tensor", None),
            P("expert", None, None, "tensor"),
            P("expert", "tensor", None),
            P("expert", None, None, "tensor"),
            P("expert", "tensor", None),
        ),
        check_vma=False,
    )
```
